256 devices in a mesh: row: 8 (over z), col: 32 (over y, x, core).
Axes of the slice: x: 4, y: 4, z: 8, core: 2. Of those that a mesh axis runs over, the one named last changes fastest.
Arguments:
- hidden_in: bfloat16 [3072, 2, 7168], P('row', None, 'col'), may hold values from -16 to 16
- final_gain: float32 [2, 7168], P(None, 'col'), may hold values from 0.25 to 1.75
- unembed: bfloat16 [7168, 32768], P('row', 'col'), may hold values from -2 to 2
- lengths: int32 [16], replicated, may hold values from 1 to 768, 3072 in all
- targets: int32 [3072], P('row'), may hold values from 0 to 32767
- owner: int32 [16], replicated, may hold values from 0 to 31
Outputs:
- owner_table: float32 [32, 3, 16], P('col')
The draws below stay inside these ranges and needn't reach their ends.
Inputs may be any that keep to these rules, and one draw needn't show every extreme that they name: The lengths sum to 3072; the longest is exactly 768.
All inputs are finite; a program needn't handle non-finite values.
Results may differ from the reference program's by a relative error of at most 0.00056.
Values may be sent and summed in bfloat16 or wider, within the bound.
No kernel may reach another device: no remote copies, remote signals or barrier semaphores. Data moves between devices by JAX's collectives and lax.ppermute only.
A program may use at most 128 MiB of HBM per device.

```python
import math
import jax
import jax.numpy as jnp
import numpy as np
from jax import lax

D = 7168
VOCAB = 32768
TOK_ROW = 384
TOKENS = 3072
MOST = 768
SEQS = 16
N_COL = 32


def draw_hidden_in(key, part):
    noise_key, row_key, col_key = jax.random.split(key, 3)
    full_shape = (TOKENS, 2, D)
    base_draw = jax.random.normal(noise_key, full_shape, jnp.float32)
    row_scale = jnp.exp(jax.random.uniform(row_key, (TOKENS, 2, 1), jnp.float32, -1.15, 1.15))
    ramp_up = jnp.exp(math.log(3.0) * (jnp.arange(D, dtype=jnp.float32) / D - 0.5))
    col_scale = ramp_up[None, None, :] * jnp.exp(jax.random.uniform(col_key, (1, 2, D), jnp.float32, -0.35, 0.35))
    return jnp.clip(base_draw * row_scale * col_scale, -16.0, 16.0).astype(jnp.bfloat16)


def draw_unembed(key, part):
    base_key = jax.random.fold_in(key, 0)
    ramp_up = jnp.exp(math.log(1.7) * (jnp.arange(VOCAB, dtype=jnp.float32) / VOCAB - 0.5))
    base_draw = jax.random.normal(base_key, (D, VOCAB), jnp.float32) * (3.0 / math.sqrt(D)) * ramp_up[None, :]
    return jnp.clip(base_draw, -2.0, 2.0).astype(jnp.bfloat16)


def plant(result, stream_key, low, top_value):
    spot = [jax.random.randint(jax.random.fold_in(stream_key, axis), (), 0, length) for axis, length in enumerate(result.shape)]
    main_axis = result.shape.index(max(result.shape))
    beside = spot[:main_axis] + [(spot[main_axis] + 1) % result.shape[main_axis]] + spot[main_axis + 1:]
    return result.at[tuple(spot)].set(low).at[tuple(beside)].set(top_value)


def rank_bounds(count, slope):
    weights = [(1 << 20) // math.isqrt(standing ** slope) + 1 for standing in range(1, count + 1)]
    spread = 1 + sum(weights) // (1 << 30)
    return np.cumsum(np.array([max(1, weight // spread) for weight in weights]))


def ranked_ids(stream_key, shape, count, slope):
    listing = rank_bounds(count, slope)
    pick = jax.random.randint(jax.random.fold_in(stream_key, 1), shape, 0, int(listing[count - 1]))
    rank = jnp.searchsorted(jnp.asarray(listing, jnp.int32), pick, side="right")
    return jax.random.permutation(jax.random.fold_in(stream_key, 2), count)[rank].astype(jnp.int32)


def profile(count, total, bound, lean):
    portions = [(1 << 20) // math.isqrt(grade ** lean) + 1 for grade in range(2, count + 1)]
    spare, given = total - bound - (count - 1), [1] * (count - 1)
    while spare > 0:
        candidates = [i for i in range(count - 1) if given[i] < bound]
        pool, remaining = sum([portions[i] for i in candidates]), spare
        for i in candidates:
            more = min(bound - given[i], max(1, remaining * portions[i] // pool), spare)
            given[i] = given[i] + more
            spare = spare - more
    return np.array([bound] + given)


def uneven_parts(stream_key, amount, total, bound, slope):
    if amount == 2:
        one = jax.random.randint(stream_key, (), max(1, total - bound), min(bound, total - 1) + 1)
        return jnp.stack([one, total - one])
    tallies = jnp.asarray(profile(amount, total, bound, slope), jnp.int32)
    twos = (amount - 1) // 2
    donor, receiver = tallies[1:1 + 2 * twos:2], tallies[2:2 + 2 * twos:2]
    margin = jnp.minimum(donor - 1, bound - receiver)
    passed = jax.random.randint(jax.random.fold_in(stream_key, 1), (twos,), 0, 1 << 20) % (margin + 1)
    tallies = tallies.at[1:1 + 2 * twos:2].set(donor - passed).at[2:2 + 2 * twos:2].set(receiver + passed)
    return tallies[jax.random.permutation(jax.random.fold_in(stream_key, 2), amount)]


def setup_inputs(seed: int = 0) -> dict:
    key_of = jax.random.split(jax.random.key(seed), 7)
    return {
        "hidden_in": draw_hidden_in(jax.random.fold_in(key_of[6], 71), 0),
        "final_gain": jnp.clip(1.0 + 0.15 * jax.random.normal(key_of[1], (2, D), jnp.float32), 0.25, 1.75),
        "unembed": draw_unembed(jax.random.fold_in(key_of[6], 71), 0),
        "lengths": uneven_parts(key_of[3], SEQS, TOKENS, MOST, 1).astype(jnp.int32),
        "targets": plant(ranked_ids(key_of[4], (TOKENS,), VOCAB, 2), jax.random.fold_in(key_of[4], 3), 0, VOCAB - 1).astype(jnp.int32),
        "owner": plant(jax.random.randint(key_of[5], (SEQS,), 0, N_COL), jax.random.fold_in(key_of[5], 1), 0, N_COL - 1).astype(jnp.int32),
    }


EPS = 1e-05

def reference(hidden_in, final_gain, unembed, lengths, targets, owner):
    stream = hidden_in.astype(jnp.float32)
    normed = (stream * lax.rsqrt(lax.optimization_barrier(jnp.mean(stream * stream, axis=2, keepdims=True)) + EPS) * final_gain[None, :, :]).astype(jnp.bfloat16)
    block_count = TOKENS // TOK_ROW
    vocab_ids = jnp.arange(VOCAB, dtype=jnp.int32)

    def score(inputs):
        block_rows, block_targets = inputs
        results = []
        for model_index in range(2):
            logits = jnp.dot(block_rows[:, model_index], unembed, preferred_element_type=jnp.float32)
            row_max = lax.optimization_barrier(jnp.max(logits, axis=1))
            exp_total = lax.optimization_barrier(jnp.sum(jnp.exp(logits - row_max[:, None]), axis=1))
            picked = lax.optimization_barrier(jnp.sum(jnp.where(block_targets[:, None] == vocab_ids[None, :], logits, 0.0), axis=1))
            results.append(picked - (row_max + jnp.log(exp_total)))
        return results[0] - results[1]
    log_ratio = lax.map(score, (normed.reshape(block_count, TOK_ROW, 2, D), targets.reshape(block_count, TOK_ROW))).reshape(TOKENS)
    token_index = jnp.arange(TOKENS, dtype=jnp.int32)
    seq_ends = jnp.cumsum(lengths).astype(jnp.int32)
    segment = lax.optimization_barrier(jnp.sum((seq_ends[None, :] <= token_index[:, None]).astype(jnp.int32), axis=1))
    member = segment[:, None] == jnp.arange(SEQS, dtype=jnp.int32)[None, :]
    ratio_sums = lax.optimization_barrier(jnp.sum(jnp.where(member, log_ratio[:, None], 0.0), axis=0))
    squares = lax.optimization_barrier(jnp.sum(jnp.where(member, (log_ratio * log_ratio)[:, None], 0.0), axis=0))
    ratio_max = lax.optimization_barrier(jnp.max(jnp.where(member, log_ratio[:, None], -1e+30), axis=0))
    seq_stats = jnp.stack([ratio_sums, squares, ratio_max])
    owned = owner[None, :] == jnp.arange(N_COL, dtype=jnp.int32)[:, None]
    return jnp.where(owned[:, None, :], seq_stats[None], 0.0)
```

```python
import jax
import jax.numpy as jnp
from jax import lax
from jax.sharding import PartitionSpec as P

D = 7168


EPS = 1e-05


def per_device(hidden_in, final_gain, unembed, lengths, targets, owner):
    tok_rows = hidden_in.shape[0]
    vocab_cols = unembed.shape[1]
    col_index = lax.axis_index("col")
    row_index = lax.axis_index("row")
    full_unembed = lax.all_gather(unembed, "row", axis=0, tiled=True)
    full_hidden = lax.all_gather(hidden_in, "col", axis=2, tiled=True)
    full_gain = lax.all_gather(final_gain, "col", axis=1, tiled=True)
    stream = full_hidden.astype(jnp.float32)
    mean_square = jnp.sum(stream * stream, axis=2) / D
    features = (stream * lax.rsqrt(mean_square[:, :, None] + EPS) * full_gain[None, :, :]).astype(
        jnp.bfloat16
    )
    logits = jnp.einsum(
        "tmd,dv->tmv", features, full_unembed, preferred_element_type=jnp.float32
    )
    row_max = jnp.max(logits, axis=2)
    exp_total = jnp.sum(jnp.exp(logits - row_max[:, :, None]), axis=2)
    vocab_ids = col_index * vocab_cols + jnp.arange(vocab_cols, dtype=jnp.int32)
    picked = jnp.sum(
        jnp.where(targets[:, None, None] == vocab_ids[None, None, :], logits, 0.0), axis=2
    )
    parts = lax.all_gather(jnp.stack([row_max, exp_total, picked]), "col")
    max_logit = jnp.max(parts[:, 0], axis=0)
    exp_total = jnp.sum(parts[:, 1] * jnp.exp(parts[:, 0] - max_logit[None]), axis=0)
    picked = jnp.sum(parts[:, 2], axis=0)
    logp = picked - (max_logit + jnp.log(exp_total))
    log_ratio = logp[:, 0] - logp[:, 1]
    token_index = row_index * tok_rows + jnp.arange(tok_rows, dtype=jnp.int32)
    seq_ends = jnp.cumsum(lengths)
    segment = jnp.sum((seq_ends[None, :] <= token_index[:, None]).astype(jnp.int32), axis=1)
    member = segment[:, None] == jnp.arange(lengths.shape[0], dtype=jnp.int32)[None, :]
    ratio_sums = jnp.sum(jnp.where(member, log_ratio[:, None], 0.0), axis=0)
    squares = jnp.sum(jnp.where(member, (log_ratio * log_ratio)[:, None], 0.0), axis=0)
    ratio_max = jnp.max(jnp.where(member, log_ratio[:, None], -1e30), axis=0)
    stats = lax.all_gather(jnp.stack([ratio_sums, squares, ratio_max]), "row")
    seq_stats = jnp.stack(
        [jnp.sum(stats[:, 0], axis=0), jnp.sum(stats[:, 1], axis=0), jnp.max(stats[:, 2], axis=0)]
    )
    owned = owner == col_index
    return jnp.where(owned[None, :], seq_stats, 0.0)[None]


def solution(mesh):
    in_specs = (P("row", None, "col"), P(None, "col"), P("row", "col"), P(), P("row"), P())
    out_specs = P("col", None, None)
    return jax.shard_map(
        per_device, mesh=mesh, in_specs=in_specs, out_specs=out_specs, check_vma=False
    )
```

```python
import jax
import jax.numpy as jnp
from jax import lax
from jax.sharding import PartitionSpec as P

D = 7168


EPS = 1e-05


def per_device(hidden_in, final_gain, unembed, lengths, targets, owner):
    tok_rows = hidden_in.shape[0]
    shard_rows, vocab_cols = unembed.shape
    half = vocab_cols // 2
    n_row = lax.axis_size("row")
    col_index = lax.axis_index("col")
    row_index = lax.axis_index("row")
    full_hidden = lax.all_gather(hidden_in, "col", axis=2, tiled=True)
    full_gain = lax.all_gather(final_gain, "col", axis=1, tiled=True)
    stream = full_hidden.astype(jnp.float32)
    mean_square = jnp.sum(stream * stream, axis=2) / D
    features = (stream * lax.rsqrt(mean_square[:, :, None] + EPS) * full_gain[None, :, :]).astype(
        jnp.bfloat16
    )

    def block_logits(block, shard):
        rows = lax.dynamic_slice_in_dim(features, shard * shard_rows, shard_rows, axis=2)
        return jnp.einsum("tmd,dv->tmv", rows, block, preferred_element_type=jnp.float32)

    forward = [(i, (i + 1) % n_row) for i in range(n_row)]
    backward = [(i, (i - 1) % n_row) for i in range(n_row)]
    left, right = unembed[:, :half], unembed[:, half:]
    logits_left = block_logits(left, row_index)
    logits_right = block_logits(right, row_index)
    for step in range(1, n_row):
        left = lax.ppermute(left, "row", forward)
        right = lax.ppermute(right, "row", backward)
        logits_left = logits_left + block_logits(left, (row_index - step) % n_row)
        logits_right = logits_right + block_logits(right, (row_index + step) % n_row)
    logits = jnp.concatenate([logits_left, logits_right], axis=2)
    row_max = jnp.max(logits, axis=2)
    exp_total = jnp.sum(jnp.exp(logits - row_max[:, :, None]), axis=2)
    vocab_ids = col_index * vocab_cols + jnp.arange(vocab_cols, dtype=jnp.int32)
    picked = jnp.sum(
        jnp.where(targets[:, None, None] == vocab_ids[None, None, :], logits, 0.0), axis=2
    )
    parts = lax.all_gather(jnp.stack([row_max, exp_total, picked]), "col")
    max_logit = jnp.max(parts[:, 0], axis=0)
    exp_total = jnp.sum(parts[:, 1] * jnp.exp(parts[:, 0] - max_logit[None]), axis=0)
    picked = jnp.sum(parts[:, 2], axis=0)
    logp = picked - (max_logit + jnp.log(exp_total))
    log_ratio = logp[:, 0] - logp[:, 1]
    token_index = row_index * tok_rows + jnp.arange(tok_rows, dtype=jnp.int32)
    seq_ends = jnp.cumsum(lengths)
    segment = jnp.sum((seq_ends[None, :] <= token_index[:, None]).astype(jnp.int32), axis=1)
    member = segment[:, None] == jnp.arange(lengths.shape[0], dtype=jnp.int32)[None, :]
    ratio_sums = jnp.sum(jnp.where(member, log_ratio[:, None], 0.0), axis=0)
    squares = jnp.sum(jnp.where(member, (log_ratio * log_ratio)[:, None], 0.0), axis=0)
    ratio_max = jnp.max(jnp.where(member, log_ratio[:, None], -1e30), axis=0)
    stats = lax.all_gather(jnp.stack([ratio_sums, squares, ratio_max]), "row")
    seq_stats = jnp.stack(
        [jnp.sum(stats[:, 0], axis=0), jnp.sum(stats[:, 1], axis=0), jnp.max(stats[:, 2], axis=0)]
    )
    owned = owner == col_index
    return jnp.where(owned[None, :], seq_stats, 0.0)[None]


def solution(mesh):
    in_specs = (P("row", None, "col"), P(None, "col"), P("row", "col"), P(), P("row"), P())
    out_specs = P("col", None, None)
    return jax.shard_map(
        per_device, mesh=mesh, in_specs=in_specs, out_specs=out_specs, check_vma=False
    )
```

```python
import jax
import jax.numpy as jnp
from jax import lax
from jax.sharding import PartitionSpec as P

D = 7168


EPS = 1e-05


def per_device(hidden_in, final_gain, unembed, lengths, targets, owner):
    tok_rows = hidden_in.shape[0]
    shard_rows, vocab_cols = unembed.shape
    half = vocab_cols // 2
    n_row = lax.axis_size("row")
    col_index = lax.axis_index("col")
    row_index = lax.axis_index("row")
    full_hidden = lax.all_gather(hidden_in, "col", axis=2, tiled=True)
    full_gain = lax.all_gather(final_gain, "col", axis=1, tiled=True)
    stream = full_hidden.astype(jnp.float32)
    mean_square = jnp.sum(stream * stream, axis=2) / D
    features = (stream * lax.rsqrt(mean_square[:, :, None] + EPS) * full_gain[None, :, :]).astype(
        jnp.bfloat16
    )
    features = features.reshape(tok_rows, 2, n_row, shard_rows).transpose(2, 0, 1, 3)

    def block_logits(block, shard):
        return jnp.einsum("tmd,dv->tmv", features[shard], block, preferred_element_type=jnp.float32)

    forward = [(i, (i + 1) % n_row) for i in range(n_row)]
    backward = [(i, (i - 1) % n_row) for i in range(n_row)]
    left, right = unembed[:, :half], unembed[:, half:]
    logits_left = block_logits(left, row_index)
    logits_right = block_logits(right, row_index)
    for step in range(1, n_row):
        left = lax.ppermute(left, "row", forward)
        right = lax.ppermute(right, "row", backward)
        logits_left = logits_left + block_logits(left, (row_index - step) % n_row)
        logits_right = logits_right + block_logits(right, (row_index + step) % n_row)
    logits = jnp.concatenate([logits_left, logits_right], axis=2)
    row_max = jnp.max(logits, axis=2)
    exp_total = jnp.sum(jnp.exp(logits - row_max[:, :, None]), axis=2)
    vocab_ids = col_index * vocab_cols + jnp.arange(vocab_cols, dtype=jnp.int32)
    picked = jnp.sum(
        jnp.where(targets[:, None, None] == vocab_ids[None, None, :], logits, 0.0), axis=2
    )
    n_col = lax.axis_size("col")
    parts = lax.all_gather(jnp.stack([row_max, exp_total, picked]), ("row", "col"))
    parts = parts.reshape(n_row, n_col, 3, tok_rows, 2)
    max_logit = jnp.max(parts[:, :, 0], axis=1)
    exp_total = jnp.sum(parts[:, :, 1] * jnp.exp(parts[:, :, 0] - max_logit[:, None]), axis=1)
    picked = jnp.sum(parts[:, :, 2], axis=1)
    logp = picked - (max_logit + jnp.log(exp_total))
    log_ratio = (logp[:, :, 0] - logp[:, :, 1]).reshape(n_row * tok_rows)
    token_index = jnp.arange(n_row * tok_rows, dtype=jnp.int32)
    seq_ends = jnp.cumsum(lengths)
    segment = jnp.sum((seq_ends[None, :] <= token_index[:, None]).astype(jnp.int32), axis=1)
    member = segment[:, None] == jnp.arange(lengths.shape[0], dtype=jnp.int32)[None, :]
    ratio_sums = jnp.sum(jnp.where(member, log_ratio[:, None], 0.0), axis=0)
    squares = jnp.sum(jnp.where(member, (log_ratio * log_ratio)[:, None], 0.0), axis=0)
    ratio_max = jnp.max(jnp.where(member, log_ratio[:, None], -1e30), axis=0)
    seq_stats = jnp.stack([ratio_sums, squares, ratio_max])
    owned = owner == col_index
    return jnp.where(owned[None, :], seq_stats, 0.0)[None]


def solution(mesh):
    in_specs = (P("row", None, "col"), P(None, "col"), P("row", "col"), P(), P("row"), P())
    out_specs = P("col", None, None)
    return jax.shard_map(
        per_device, mesh=mesh, in_specs=in_specs, out_specs=out_specs, check_vma=False
    )
```

```python
import jax
import jax.numpy as jnp
from jax import lax
from jax.sharding import PartitionSpec as P

D = 7168


EPS = 1e-05


def per_device(hidden_in, final_gain, unembed, lengths, targets, owner):
    tok_rows = hidden_in.shape[0]
    shard_rows, vocab_cols = unembed.shape
    half = vocab_cols // 2
    n_row = lax.axis_size("row")
    col_index = lax.axis_index("col")
    row_index = lax.axis_index("row")
    full_hidden = lax.all_gather(hidden_in, "col", axis=2, tiled=True)
    full_gain = lax.all_gather(final_gain, "col", axis=1, tiled=True)
    stream = full_hidden.astype(jnp.float32)
    mean_square = jnp.sum(stream * stream, axis=2) / D
    features = (stream * lax.rsqrt(mean_square[:, :, None] + EPS) * full_gain[None, :, :]).astype(
        jnp.bfloat16
    )
    features = features.reshape(tok_rows, 2, n_row, shard_rows).transpose(2, 0, 1, 3)

    def block_logits(block, shard):
        return jnp.einsum("tmd,dv->tmv", features[shard], block, preferred_element_type=jnp.float32)

    forward = [(i, (i + 1) % n_row) for i in range(n_row)]
    backward = [(i, (i - 1) % n_row) for i in range(n_row)]
    left, right = unembed[:, :half], unembed[:, half:]
    logits_left = block_logits(left, row_index)
    logits_right = block_logits(right, row_index)
    for step in range(1, n_row):
        left = lax.ppermute(left, "row", forward)
        right = lax.ppermute(right, "row", backward)
        logits_left = logits_left + block_logits(left, (row_index - step) % n_row)
        logits_right = logits_right + block_logits(right, (row_index + step) % n_row)
    logits = jnp.concatenate([logits_left, logits_right], axis=2)
    row_max = jnp.max(logits, axis=2)
    exp_total = jnp.sum(jnp.exp(logits - row_max[:, :, None]), axis=2)
    vocab_ids = col_index * vocab_cols + jnp.arange(vocab_cols, dtype=jnp.int32)
    picked = jnp.sum(
        jnp.where(targets[:, None, None] == vocab_ids[None, None, :], logits, 0.0), axis=2
    )
    parts = lax.all_gather(jnp.stack([row_max, exp_total, picked]), "col")
    max_logit = jnp.max(parts[:, 0], axis=0)
    exp_total = jnp.sum(parts[:, 1] * jnp.exp(parts[:, 0] - max_logit[None]), axis=0)
    picked = jnp.sum(parts[:, 2], axis=0)
    logp = picked - (max_logit + jnp.log(exp_total))
    log_ratio = logp[:, 0] - logp[:, 1]
    token_index = row_index * tok_rows + jnp.arange(tok_rows, dtype=jnp.int32)
    seq_ends = jnp.cumsum(lengths)
    segment = jnp.sum((seq_ends[None, :] <= token_index[:, None]).astype(jnp.int32), axis=1)
    member = segment[:, None] == jnp.arange(lengths.shape[0], dtype=jnp.int32)[None, :]
    ratio_sums = jnp.sum(jnp.where(member, log_ratio[:, None], 0.0), axis=0)
    squares = jnp.sum(jnp.where(member, (log_ratio * log_ratio)[:, None], 0.0), axis=0)
    ratio_max = jnp.max(jnp.where(member, log_ratio[:, None], -1e30), axis=0)
    stats = lax.all_gather(jnp.stack([ratio_sums, squares, ratio_max]), "row")
    seq_stats = jnp.stack(
        [jnp.sum(stats[:, 0], axis=0), jnp.sum(stats[:, 1], axis=0), jnp.max(stats[:, 2], axis=0)]
    )
    owned = owner == col_index
    return jnp.where(owned[None, :], seq_stats, 0.0)[None]


def solution(mesh):
    in_specs = (P("row", None, "col"), P(None, "col"), P("row", "col"), P(), P("row"), P())
    out_specs = P("col", None, None)
    return jax.shard_map(
        per_device, mesh=mesh, in_specs=in_specs, out_specs=out_specs, check_vma=False
    )
```

```python
import jax
import jax.numpy as jnp
from jax import lax
from jax.sharding import PartitionSpec as P

D = 7168


EPS = 1e-05


def per_device(hidden_in, final_gain, unembed, lengths, targets, owner):
    tok_rows = hidden_in.shape[0]
    shard_rows, vocab_cols = unembed.shape
    half = vocab_cols // 2
    n_row = lax.axis_size("row")
    col_index = lax.axis_index("col")
    row_index = lax.axis_index("row")
    packed = jnp.concatenate([hidden_in.astype(jnp.float32), final_gain[None]], axis=0)
    full_packed = lax.all_gather(packed, "col", axis=2, tiled=True)
    stream = full_packed[:tok_rows]
    full_gain = full_packed[tok_rows]
    mean_square = jnp.sum(stream * stream, axis=2) / D
    features = (stream * lax.rsqrt(mean_square[:, :, None] + EPS) * full_gain[None, :, :]).astype(
        jnp.bfloat16
    )
    features = features.reshape(tok_rows, 2, n_row, shard_rows).transpose(2, 0, 1, 3)

    def block_logits(block, shard):
        return jnp.einsum("tmd,dv->tmv", features[shard], block, preferred_element_type=jnp.float32)

    forward = [(i, (i + 1) % n_row) for i in range(n_row)]
    backward = [(i, (i - 1) % n_row) for i in range(n_row)]
    left, right = unembed[:, :half], unembed[:, half:]
    logits_left = block_logits(left, row_index)
    logits_right = block_logits(right, row_index)
    for step in range(1, n_row):
        left = lax.ppermute(left, "row", forward)
        right = lax.ppermute(right, "row", backward)
        logits_left = logits_left + block_logits(left, (row_index - step) % n_row)
        logits_right = logits_right + block_logits(right, (row_index + step) % n_row)
    logits = jnp.concatenate([logits_left, logits_right], axis=2)
    row_max = jnp.max(logits, axis=2)
    exp_total = jnp.sum(jnp.exp(logits - row_max[:, :, None]), axis=2)
    vocab_ids = col_index * vocab_cols + jnp.arange(vocab_cols, dtype=jnp.int32)
    picked = jnp.sum(
        jnp.where(targets[:, None, None] == vocab_ids[None, None, :], logits, 0.0), axis=2
    )
    parts = lax.all_gather(jnp.stack([row_max, exp_total, picked]), "col")
    max_logit = jnp.max(parts[:, 0], axis=0)
    exp_total = jnp.sum(parts[:, 1] * jnp.exp(parts[:, 0] - max_logit[None]), axis=0)
    picked = jnp.sum(parts[:, 2], axis=0)
    logp = picked - (max_logit + jnp.log(exp_total))
    log_ratio = logp[:, 0] - logp[:, 1]
    token_index = row_index * tok_rows + jnp.arange(tok_rows, dtype=jnp.int32)
    seq_ends = jnp.cumsum(lengths)
    segment = jnp.sum((seq_ends[None, :] <= token_index[:, None]).astype(jnp.int32), axis=1)
    member = segment[:, None] == jnp.arange(lengths.shape[0], dtype=jnp.int32)[None, :]
    ratio_sums = jnp.sum(jnp.where(member, log_ratio[:, None], 0.0), axis=0)
    squares = jnp.sum(jnp.where(member, (log_ratio * log_ratio)[:, None], 0.0), axis=0)
    ratio_max = jnp.max(jnp.where(member, log_ratio[:, None], -1e30), axis=0)
    stats = lax.all_gather(jnp.stack([ratio_sums, squares, ratio_max]), "row")
    seq_stats = jnp.stack(
        [jnp.sum(stats[:, 0], axis=0), jnp.sum(stats[:, 1], axis=0), jnp.max(stats[:, 2], axis=0)]
    )
    owned = owner == col_index
    return jnp.where(owned[None, :], seq_stats, 0.0)[None]


def solution(mesh):
    in_specs = (P("row", None, "col"), P(None, "col"), P("row", "col"), P(), P("row"), P())
    out_specs = P("col", None, None)
    return jax.shard_map(
        per_device, mesh=mesh, in_specs=in_specs, out_specs=out_specs, check_vma=False
    )
```

```python
import jax
import jax.numpy as jnp
from jax import lax
from jax.sharding import PartitionSpec as P

D = 7168


EPS = 1e-05


def per_device(hidden_in, final_gain, unembed, lengths, targets, owner):
    tok_rows = hidden_in.shape[0]
    shard_rows, vocab_cols = unembed.shape
    half = vocab_cols // 2
    n_row = lax.axis_size("row")
    col_index = lax.axis_index("col")
    row_index = lax.axis_index("row")
    full_hidden = lax.all_gather(hidden_in, "col", axis=2, tiled=True)
    full_gain = lax.all_gather(final_gain, "col", axis=1, tiled=True)
    forward = [(i, (i + 1) % n_row) for i in range(n_row)]
    backward = [(i, (i - 1) % n_row) for i in range(n_row)]
    left, right = unembed[:, :half], unembed[:, half:]
    pending = [(left, right, row_index, row_index)]
    features = None
    logits_left = None
    logits_right = None

    def block_logits(block, shard):
        return jnp.einsum("tmd,dv->tmv", features[shard], block, preferred_element_type=jnp.float32)

    def add_pending(logits_left, logits_right):
        for block_left, block_right, shard_left, shard_right in pending:
            part_left = block_logits(block_left, shard_left)
            part_right = block_logits(block_right, shard_right)
            if logits_left is None:
                logits_left, logits_right = part_left, part_right
            else:
                logits_left = logits_left + part_left
                logits_right = logits_right + part_right
        return logits_left, logits_right

    for step in range(1, n_row):
        if step == 3:
            left, right, full_gain = lax.optimization_barrier((left, right, full_gain))
        if step == 5:
            stream = full_hidden.astype(jnp.float32)
            mean_square = jnp.sum(stream * stream, axis=2) / D
            features = (
                stream * lax.rsqrt(mean_square[:, :, None] + EPS) * full_gain[None, :, :]
            ).astype(jnp.bfloat16)
            features = features.reshape(tok_rows, 2, n_row, shard_rows).transpose(2, 0, 1, 3)
            left, right, features = lax.optimization_barrier((left, right, features))
        if step >= 6:
            logits_left, logits_right = add_pending(logits_left, logits_right)
            pending = []
            left, right, logits_left, logits_right = lax.optimization_barrier(
                (left, right, logits_left, logits_right)
            )
        left = lax.ppermute(left, "row", forward)
        right = lax.ppermute(right, "row", backward)
        pending.append((left, right, (row_index - step) % n_row, (row_index + step) % n_row))
    logits_left, logits_right = add_pending(logits_left, logits_right)
    logits = jnp.concatenate([logits_left, logits_right], axis=2)
    row_max = jnp.max(logits, axis=2)
    exp_total = jnp.sum(jnp.exp(logits - row_max[:, :, None]), axis=2)
    vocab_ids = col_index * vocab_cols + jnp.arange(vocab_cols, dtype=jnp.int32)
    picked = jnp.sum(
        jnp.where(targets[:, None, None] == vocab_ids[None, None, :], logits, 0.0), axis=2
    )
    parts = lax.all_gather(jnp.stack([row_max, exp_total, picked]), "col")
    max_logit = jnp.max(parts[:, 0], axis=0)
    exp_total = jnp.sum(parts[:, 1] * jnp.exp(parts[:, 0] - max_logit[None]), axis=0)
    picked = jnp.sum(parts[:, 2], axis=0)
    logp = picked - (max_logit + jnp.log(exp_total))
    log_ratio = logp[:, 0] - logp[:, 1]
    token_index = row_index * tok_rows + jnp.arange(tok_rows, dtype=jnp.int32)
    seq_ends = jnp.cumsum(lengths)
    segment = jnp.sum((seq_ends[None, :] <= token_index[:, None]).astype(jnp.int32), axis=1)
    member = segment[:, None] == jnp.arange(lengths.shape[0], dtype=jnp.int32)[None, :]
    ratio_sums = jnp.sum(jnp.where(member, log_ratio[:, None], 0.0), axis=0)
    squares = jnp.sum(jnp.where(member, (log_ratio * log_ratio)[:, None], 0.0), axis=0)
    ratio_max = jnp.max(jnp.where(member, log_ratio[:, None], -1e30), axis=0)
    stats = lax.all_gather(jnp.stack([ratio_sums, squares, ratio_max]), "row")
    seq_stats = jnp.stack(
        [jnp.sum(stats[:, 0], axis=0), jnp.sum(stats[:, 1], axis=0), jnp.max(stats[:, 2], axis=0)]
    )
    owned = owner == col_index
    return jnp.where(owned[None, :], seq_stats, 0.0)[None]


def solution(mesh):
    in_specs = (P("row", None, "col"), P(None, "col"), P("row", "col"), P(), P("row"), P())
    out_specs = P("col", None, None)
    return jax.shard_map(
        per_device, mesh=mesh, in_specs=in_specs, out_specs=out_specs, check_vma=False
    )
```

```python
import jax
import jax.numpy as jnp
from jax import lax
from jax.sharding import PartitionSpec as P

D = 7168


EPS = 1e-05


def per_device(hidden_in, final_gain, unembed, lengths, targets, owner):
    tok_rows = hidden_in.shape[0]
    shard_rows, vocab_cols = unembed.shape
    half = vocab_cols // 2
    n_row = lax.axis_size("row")
    col_index = lax.axis_index("col")
    row_index = lax.axis_index("row")
    full_hidden = lax.all_gather(hidden_in, "col", axis=2, tiled=True)
    full_gain = lax.all_gather(final_gain, "col", axis=1, tiled=True)
    forward = [(i, (i + 1) % n_row) for i in range(n_row)]
    backward = [(i, (i - 1) % n_row) for i in range(n_row)]
    left, right = unembed[:, :half], unembed[:, half:]
    pending = [(left, right, row_index, row_index)]
    features = None
    logits_left = None
    logits_right = None

    def block_logits(block, shard):
        return jnp.einsum("tmd,dv->tmv", features[shard], block, preferred_element_type=jnp.float32)

    def add_pending(logits_left, logits_right):
        for block_left, block_right, shard_left, shard_right in pending:
            part_left = block_logits(block_left, shard_left)
            part_right = block_logits(block_right, shard_right)
            if logits_left is None:
                logits_left, logits_right = part_left, part_right
            else:
                logits_left = logits_left + part_left
                logits_right = logits_right + part_right
        return logits_left, logits_right

    for step in range(1, n_row):
        if step == 3:
            left, right, full_gain = lax.optimization_barrier((left, right, full_gain))
        if step == 5:
            stream = full_hidden.astype(jnp.float32)
            mean_square = jnp.sum(stream * stream, axis=2) / D
            features = (
                stream * lax.rsqrt(mean_square[:, :, None] + EPS) * full_gain[None, :, :]
            ).astype(jnp.bfloat16)
            left, right, features = lax.optimization_barrier((left, right, features))
            features = features.reshape(tok_rows, 2, n_row, shard_rows).transpose(2, 0, 1, 3)
        if step == 7:
            logits_left, logits_right = add_pending(logits_left, logits_right)
            pending = []
            left, right, logits_left, logits_right = lax.optimization_barrier(
                (left, right, logits_left, logits_right)
            )
        left = lax.ppermute(left, "row", forward)
        right = lax.ppermute(right, "row", backward)
        pending.append((left, right, (row_index - step) % n_row, (row_index + step) % n_row))
    logits_left, logits_right = add_pending(logits_left, logits_right)
    logits = jnp.concatenate([logits_left, logits_right], axis=2)
    row_max = jnp.max(logits, axis=2)
    exp_total = jnp.sum(jnp.exp(logits - row_max[:, :, None]), axis=2)
    vocab_ids = col_index * vocab_cols + jnp.arange(vocab_cols, dtype=jnp.int32)
    picked = jnp.sum(
        jnp.where(targets[:, None, None] == vocab_ids[None, None, :], logits, 0.0), axis=2
    )
    parts = lax.all_gather(jnp.stack([row_max, exp_total, picked]), "col")
    max_logit = jnp.max(parts[:, 0], axis=0)
    exp_total = jnp.sum(parts[:, 1] * jnp.exp(parts[:, 0] - max_logit[None]), axis=0)
    picked = jnp.sum(parts[:, 2], axis=0)
    logp = picked - (max_logit + jnp.log(exp_total))
    log_ratio = logp[:, 0] - logp[:, 1]
    token_index = row_index * tok_rows + jnp.arange(tok_rows, dtype=jnp.int32)
    seq_ends = jnp.cumsum(lengths)
    segment = jnp.sum((seq_ends[None, :] <= token_index[:, None]).astype(jnp.int32), axis=1)
    member = segment[:, None] == jnp.arange(lengths.shape[0], dtype=jnp.int32)[None, :]
    ratio_sums = jnp.sum(jnp.where(member, log_ratio[:, None], 0.0), axis=0)
    squares = jnp.sum(jnp.where(member, (log_ratio * log_ratio)[:, None], 0.0), axis=0)
    ratio_max = jnp.max(jnp.where(member, log_ratio[:, None], -1e30), axis=0)
    stats = lax.all_gather(jnp.stack([ratio_sums, squares, ratio_max]), "row")
    seq_stats = jnp.stack(
        [jnp.sum(stats[:, 0], axis=0), jnp.sum(stats[:, 1], axis=0), jnp.max(stats[:, 2], axis=0)]
    )
    owned = owner == col_index
    return jnp.where(owned[None, :], seq_stats, 0.0)[None]


def solution(mesh):
    in_specs = (P("row", None, "col"), P(None, "col"), P("row", "col"), P(), P("row"), P())
    out_specs = P("col", None, None)
    return jax.shard_map(
        per_device, mesh=mesh, in_specs=in_specs, out_specs=out_specs, check_vma=False
    )
```

```python
import jax
import jax.numpy as jnp
from jax import lax
from jax.sharding import PartitionSpec as P

D = 7168


EPS = 1e-05


def per_device(hidden_in, final_gain, unembed, lengths, targets, owner):
    tok_rows = hidden_in.shape[0]
    shard_rows, vocab_cols = unembed.shape
    half = vocab_cols // 2
    n_row = lax.axis_size("row")
    col_index = lax.axis_index("col")
    row_index = lax.axis_index("row")
    full_hidden = lax.all_gather(hidden_in, "col", axis=2, tiled=True)
    full_gain = lax.all_gather(final_gain, "col", axis=1, tiled=True)
    forward = [(i, (i + 1) % n_row) for i in range(n_row)]
    backward = [(i, (i - 1) % n_row) for i in range(n_row)]
    left, right = unembed[:, :half], unembed[:, half:]
    pending = [(left, right, row_index, row_index)]
    features = None
    logits_left = None
    logits_right = None

    def block_logits(block, shard):
        return jnp.einsum("tmd,dv->tmv", features[shard], block, preferred_element_type=jnp.float32)

    def add_pending(logits_left, logits_right):
        for block_left, block_right, shard_left, shard_right in pending:
            part_left = block_logits(block_left, shard_left)
            part_right = block_logits(block_right, shard_right)
            if logits_left is None:
                logits_left, logits_right = part_left, part_right
            else:
                logits_left = logits_left + part_left
                logits_right = logits_right + part_right
        return logits_left, logits_right

    for step in range(1, n_row):
        if step == 3:
            left, right, full_gain = lax.optimization_barrier((left, right, full_gain))
        if step == 5:
            stream = full_hidden.astype(jnp.float32)
            mean_square = jnp.sum(stream * stream, axis=2) / D
            features = (
                stream * lax.rsqrt(mean_square[:, :, None] + EPS) * full_gain[None, :, :]
            ).astype(jnp.bfloat16)
            left, right, features = lax.optimization_barrier((left, right, features))
            features = features.reshape(tok_rows, 2, n_row, shard_rows).transpose(2, 0, 1, 3)
        left = lax.ppermute(left, "row", forward)
        right = lax.ppermute(right, "row", backward)
        pending.append((left, right, (row_index - step) % n_row, (row_index + step) % n_row))
    logits_left, logits_right = add_pending(logits_left, logits_right)
    logits = jnp.concatenate([logits_left, logits_right], axis=2)
    row_max = jnp.max(logits, axis=2)
    exp_total = jnp.sum(jnp.exp(logits - row_max[:, :, None]), axis=2)
    vocab_ids = col_index * vocab_cols + jnp.arange(vocab_cols, dtype=jnp.int32)
    picked = jnp.sum(
        jnp.where(targets[:, None, None] == vocab_ids[None, None, :], logits, 0.0), axis=2
    )
    parts = lax.all_gather(jnp.stack([row_max, exp_total, picked]), "col")
    max_logit = jnp.max(parts[:, 0], axis=0)
    exp_total = jnp.sum(parts[:, 1] * jnp.exp(parts[:, 0] - max_logit[None]), axis=0)
    picked = jnp.sum(parts[:, 2], axis=0)
    logp = picked - (max_logit + jnp.log(exp_total))
    log_ratio = logp[:, 0] - logp[:, 1]
    token_index = row_index * tok_rows + jnp.arange(tok_rows, dtype=jnp.int32)
    seq_ends = jnp.cumsum(lengths)
    segment = jnp.sum((seq_ends[None, :] <= token_index[:, None]).astype(jnp.int32), axis=1)
    member = segment[:, None] == jnp.arange(lengths.shape[0], dtype=jnp.int32)[None, :]
    ratio_sums = jnp.sum(jnp.where(member, log_ratio[:, None], 0.0), axis=0)
    squares = jnp.sum(jnp.where(member, (log_ratio * log_ratio)[:, None], 0.0), axis=0)
    ratio_max = jnp.max(jnp.where(member, log_ratio[:, None], -1e30), axis=0)
    own_slot = (jnp.arange(n_row, dtype=jnp.int32) == row_index)[:, None, None]
    own_stats = jnp.stack([ratio_sums, squares, ratio_max])[None]
    stats = lax.psum(jnp.where(own_slot, own_stats, 0.0), "row")
    seq_stats = jnp.stack(
        [jnp.sum(stats[:, 0], axis=0), jnp.sum(stats[:, 1], axis=0), jnp.max(stats[:, 2], axis=0)]
    )
    owned = owner == col_index
    return jnp.where(owned[None, :], seq_stats, 0.0)[None]


def solution(mesh):
    in_specs = (P("row", None, "col"), P(None, "col"), P("row", "col"), P(), P("row"), P())
    out_specs = P("col", None, None)
    return jax.shard_map(
        per_device, mesh=mesh, in_specs=in_specs, out_specs=out_specs, check_vma=False
    )
```

```python
import jax
import jax.numpy as jnp
from jax import lax
from jax.sharding import PartitionSpec as P

D = 7168


EPS = 1e-05


def per_device(hidden_in, final_gain, unembed, lengths, targets, owner):
    tok_rows = hidden_in.shape[0]
    shard_rows, vocab_cols = unembed.shape
    half = vocab_cols // 2
    n_row = lax.axis_size("row")
    col_index = lax.axis_index("col")
    row_index = lax.axis_index("row")
    full_hidden = lax.all_gather(hidden_in, "col", axis=2, tiled=True)
    full_gain = lax.all_gather(final_gain, "col", axis=1, tiled=True)
    stream = full_hidden.astype(jnp.float32)
    mean_square = jnp.sum(stream * stream, axis=2) / D
    features = (stream * lax.rsqrt(mean_square[:, :, None] + EPS) * full_gain[None, :, :]).astype(
        jnp.bfloat16
    )
    features = features.reshape(tok_rows, 2, n_row, shard_rows).transpose(2, 0, 1, 3)

    def block_logits(block, shard):
        return jnp.einsum("tmd,dv->tmv", features[shard], block, preferred_element_type=jnp.float32)

    forward = [(i, (i + 1) % n_row) for i in range(n_row)]
    backward = [(i, (i - 1) % n_row) for i in range(n_row)]
    left, right = unembed[:, :half], unembed[:, half:]
    logits_left = block_logits(left, row_index)
    logits_right = block_logits(right, row_index)
    for step in range(1, n_row):
        left = lax.ppermute(left, "row", forward)
        right = lax.ppermute(right, "row", backward)
        logits_left = logits_left + block_logits(left, (row_index - step) % n_row)
        logits_right = logits_right + block_logits(right, (row_index + step) % n_row)
    logits = jnp.concatenate([logits_left, logits_right], axis=2)
    row_max = jnp.max(logits, axis=2)
    exp_total = jnp.sum(jnp.exp(logits - row_max[:, :, None]), axis=2)
    vocab_ids = col_index * vocab_cols + jnp.arange(vocab_cols, dtype=jnp.int32)
    picked = jnp.sum(
        jnp.where(targets[:, None, None] == vocab_ids[None, None, :], logits, 0.0), axis=2
    )
    parts = lax.all_gather(jnp.stack([row_max, exp_total, picked] * 4), "col")
    max_logit = jnp.max(parts[:, 0], axis=0)
    exp_total = jnp.sum(parts[:, 1] * jnp.exp(parts[:, 0] - max_logit[None]), axis=0)
    picked = jnp.sum(parts[:, 2], axis=0)
    logp = picked - (max_logit + jnp.log(exp_total))
    log_ratio = logp[:, 0] - logp[:, 1]
    token_index = row_index * tok_rows + jnp.arange(tok_rows, dtype=jnp.int32)
    seq_ends = jnp.cumsum(lengths)
    segment = jnp.sum((seq_ends[None, :] <= token_index[:, None]).astype(jnp.int32), axis=1)
    member = segment[:, None] == jnp.arange(lengths.shape[0], dtype=jnp.int32)[None, :]
    ratio_sums = jnp.sum(jnp.where(member, log_ratio[:, None], 0.0), axis=0)
    squares = jnp.sum(jnp.where(member, (log_ratio * log_ratio)[:, None], 0.0), axis=0)
    ratio_max = jnp.max(jnp.where(member, log_ratio[:, None], -1e30), axis=0)
    stats = lax.all_gather(jnp.stack([ratio_sums, squares, ratio_max]), "row")
    seq_stats = jnp.stack(
        [jnp.sum(stats[:, 0], axis=0), jnp.sum(stats[:, 1], axis=0), jnp.max(stats[:, 2], axis=0)]
    )
    owned = owner == col_index
    return jnp.where(owned[None, :], seq_stats, 0.0)[None]


def solution(mesh):
    in_specs = (P("row", None, "col"), P(None, "col"), P("row", "col"), P(), P("row"), P())
    out_specs = P("col", None, None)
    return jax.shard_map(
        per_device, mesh=mesh, in_specs=in_specs, out_specs=out_specs, check_vma=False
    )
```

```python
import jax
import jax.numpy as jnp
from jax import lax
from jax.sharding import PartitionSpec as P

D = 7168


EPS = 1e-05


def per_device(hidden_in, final_gain, unembed, lengths, targets, owner):
    tok_rows = hidden_in.shape[0]
    shard_rows, vocab_cols = unembed.shape
    half = vocab_cols // 2
    n_row = lax.axis_size("row")
    col_index = lax.axis_index("col")
    row_index = lax.axis_index("row")
    full_hidden = lax.all_gather(hidden_in, "col", axis=2, tiled=True)
    full_gain = lax.all_gather(final_gain, "col", axis=1, tiled=True)
    forward = [(i, (i + 1) % n_row) for i in range(n_row)]
    backward = [(i, (i - 1) % n_row) for i in range(n_row)]
    left, right = unembed[:, :half], unembed[:, half:]
    pending = [(left, right, row_index, row_index)]
    features = None
    logits_left = None
    logits_right = None

    def block_logits(block, shard):
        return jnp.einsum("tmd,dv->tmv", features[shard], block, preferred_element_type=jnp.float32)

    def add_pending(logits_left, logits_right):
        for block_left, block_right, shard_left, shard_right in pending:
            part_left = block_logits(block_left, shard_left)
            part_right = block_logits(block_right, shard_right)
            if logits_left is None:
                logits_left, logits_right = part_left, part_right
            else:
                logits_left = logits_left + part_left
                logits_right = logits_right + part_right
        return logits_left, logits_right

    for step in range(1, n_row):
        if step == 3:
            left, right, full_gain = lax.optimization_barrier((left, right, full_gain))
        if step == 5:
            stream = full_hidden.astype(jnp.float32)
            mean_square = jnp.sum(stream * stream, axis=2) / D
            features = (
                stream * lax.rsqrt(mean_square[:, :, None] + EPS) * full_gain[None, :, :]
            ).astype(jnp.bfloat16)
            left, right, features = lax.optimization_barrier((left, right, features))
        if step == n_row - 1:
            left, right, features = lax.optimization_barrier((left, right, features))
            features = features.reshape(tok_rows, 2, n_row, shard_rows).transpose(2, 0, 1, 3)
        left = lax.ppermute(left, "row", forward)
        right = lax.ppermute(right, "row", backward)
        pending.append((left, right, (row_index - step) % n_row, (row_index + step) % n_row))
    logits_left, logits_right = add_pending(logits_left, logits_right)
    logits = jnp.concatenate([logits_left, logits_right], axis=2)
    row_max = jnp.max(logits, axis=2)
    exp_total = jnp.sum(jnp.exp(logits - row_max[:, :, None]), axis=2)
    vocab_ids = col_index * vocab_cols + jnp.arange(vocab_cols, dtype=jnp.int32)
    picked = jnp.sum(
        jnp.where(targets[:, None, None] == vocab_ids[None, None, :], logits, 0.0), axis=2
    )
    parts = lax.all_gather(jnp.stack([row_max, exp_total, picked]), "col")
    max_logit = jnp.max(parts[:, 0], axis=0)
    exp_total = jnp.sum(parts[:, 1] * jnp.exp(parts[:, 0] - max_logit[None]), axis=0)
    picked = jnp.sum(parts[:, 2], axis=0)
    logp = picked - (max_logit + jnp.log(exp_total))
    log_ratio = logp[:, 0] - logp[:, 1]
    token_index = row_index * tok_rows + jnp.arange(tok_rows, dtype=jnp.int32)
    seq_ends = jnp.cumsum(lengths)
    segment = jnp.sum((seq_ends[None, :] <= token_index[:, None]).astype(jnp.int32), axis=1)
    member = segment[:, None] == jnp.arange(lengths.shape[0], dtype=jnp.int32)[None, :]
    ratio_sums = jnp.sum(jnp.where(member, log_ratio[:, None], 0.0), axis=0)
    squares = jnp.sum(jnp.where(member, (log_ratio * log_ratio)[:, None], 0.0), axis=0)
    ratio_max = jnp.max(jnp.where(member, log_ratio[:, None], -1e30), axis=0)
    stats = lax.all_gather(jnp.stack([ratio_sums, squares, ratio_max]), "row")
    seq_stats = jnp.stack(
        [jnp.sum(stats[:, 0], axis=0), jnp.sum(stats[:, 1], axis=0), jnp.max(stats[:, 2], axis=0)]
    )
    owned = owner == col_index
    return jnp.where(owned[None, :], seq_stats, 0.0)[None]


def solution(mesh):
    in_specs = (P("row", None, "col"), P(None, "col"), P("row", "col"), P(), P("row"), P())
    out_specs = P("col", None, None)
    return jax.shard_map(
        per_device, mesh=mesh, in_specs=in_specs, out_specs=out_specs, check_vma=False
    )
```

```python
import jax
import jax.numpy as jnp
from jax import lax
from jax.sharding import PartitionSpec as P

D = 7168


EPS = 1e-05


def per_device(hidden_in, final_gain, unembed, lengths, targets, owner):
    tok_rows = hidden_in.shape[0]
    shard_rows, vocab_cols = unembed.shape
    half = vocab_cols // 2
    n_row = lax.axis_size("row")
    col_index = lax.axis_index("col")
    row_index = lax.axis_index("row")
    full_hidden = lax.all_gather(hidden_in, "col", axis=2, tiled=True)
    full_gain = lax.all_gather(final_gain, "col", axis=1, tiled=True)
    forward = [(i, (i + 1) % n_row) for i in range(n_row)]
    backward = [(i, (i - 1) % n_row) for i in range(n_row)]
    left, right = unembed[:, :half], unembed[:, half:]
    pending = [(left, right, row_index, row_index)]
    features = None
    logits_left = None
    logits_right = None

    def block_logits(block, shard):
        return jnp.einsum("tmd,dv->tmv", features[shard], block, preferred_element_type=jnp.float32)

    def add_pending(logits_left, logits_right):
        for block_left, block_right, shard_left, shard_right in pending:
            part_left = block_logits(block_left, shard_left)
            part_right = block_logits(block_right, shard_right)
            if logits_left is None:
                logits_left, logits_right = part_left, part_right
            else:
                logits_left = logits_left + part_left
                logits_right = logits_right + part_right
        return logits_left, logits_right

    for step in range(1, n_row):
        if step == 3:
            left, right, full_gain = lax.optimization_barrier((left, right, full_gain))
        if step == 5:
            stream = full_hidden.astype(jnp.float32)
            mean_square = jnp.sum(stream * stream, axis=2) / D
            features = (
                stream * lax.rsqrt(mean_square[:, :, None] + EPS) * full_gain[None, :, :]
            ).astype(jnp.bfloat16)
            left, right, features = lax.optimization_barrier((left, right, features))
        if step == n_row - 1:
            left, right, features = lax.optimization_barrier((left, right, features))
            features = features.reshape(tok_rows, 2, n_row, shard_rows).transpose(2, 0, 1, 3)
        left, right = lax.optimization_barrier((left, right))
        left = lax.ppermute(left, "row", forward)
        right = lax.ppermute(right, "row", backward)
        pending.append((left, right, (row_index - step) % n_row, (row_index + step) % n_row))
    logits_left, logits_right = add_pending(logits_left, logits_right)
    logits = jnp.concatenate([logits_left, logits_right], axis=2)
    row_max = jnp.max(logits, axis=2)
    exp_total = jnp.sum(jnp.exp(logits - row_max[:, :, None]), axis=2)
    vocab_ids = col_index * vocab_cols + jnp.arange(vocab_cols, dtype=jnp.int32)
    picked = jnp.sum(
        jnp.where(targets[:, None, None] == vocab_ids[None, None, :], logits, 0.0), axis=2
    )
    parts = lax.all_gather(jnp.stack([row_max, exp_total, picked]), "col")
    max_logit = jnp.max(parts[:, 0], axis=0)
    exp_total = jnp.sum(parts[:, 1] * jnp.exp(parts[:, 0] - max_logit[None]), axis=0)
    picked = jnp.sum(parts[:, 2], axis=0)
    logp = picked - (max_logit + jnp.log(exp_total))
    log_ratio = logp[:, 0] - logp[:, 1]
    token_index = row_index * tok_rows + jnp.arange(tok_rows, dtype=jnp.int32)
    seq_ends = jnp.cumsum(lengths)
    segment = jnp.sum((seq_ends[None, :] <= token_index[:, None]).astype(jnp.int32), axis=1)
    member = segment[:, None] == jnp.arange(lengths.shape[0], dtype=jnp.int32)[None, :]
    ratio_sums = jnp.sum(jnp.where(member, log_ratio[:, None], 0.0), axis=0)
    squares = jnp.sum(jnp.where(member, (log_ratio * log_ratio)[:, None], 0.0), axis=0)
    ratio_max = jnp.max(jnp.where(member, log_ratio[:, None], -1e30), axis=0)
    stats = lax.all_gather(jnp.stack([ratio_sums, squares, ratio_max]), "row")
    seq_stats = jnp.stack(
        [jnp.sum(stats[:, 0], axis=0), jnp.sum(stats[:, 1], axis=0), jnp.max(stats[:, 2], axis=0)]
    )
    owned = owner == col_index
    return jnp.where(owned[None, :], seq_stats, 0.0)[None]


def solution(mesh):
    in_specs = (P("row", None, "col"), P(None, "col"), P("row", "col"), P(), P("row"), P())
    out_specs = P("col", None, None)
    return jax.shard_map(
        per_device, mesh=mesh, in_specs=in_specs, out_specs=out_specs, check_vma=False
    )
```

```python
import jax
import jax.numpy as jnp
from jax import lax
from jax.sharding import PartitionSpec as P

D = 7168


EPS = 1e-05


def per_device(hidden_in, final_gain, unembed, lengths, targets, owner):
    tok_rows = hidden_in.shape[0]
    shard_rows, vocab_cols = unembed.shape
    half = vocab_cols // 2
    n_row = lax.axis_size("row")
    col_index = lax.axis_index("col")
    row_index = lax.axis_index("row")
    full_hidden = lax.all_gather(hidden_in, "col", axis=2, tiled=True)
    full_gain = lax.all_gather(final_gain, "col", axis=1, tiled=True)
    forward = [(i, (i + 1) % n_row) for i in range(n_row)]
    backward = [(i, (i - 1) % n_row) for i in range(n_row)]
    left, right = unembed[:, :half], unembed[:, half:]
    pending = [(left, right, row_index, row_index)]
    features = None
    logits_left = None
    logits_right = None

    def block_logits(block, shard):
        return jnp.einsum("tmd,dv->tmv", features[shard], block, preferred_element_type=jnp.float32)

    def add_pending(logits_left, logits_right):
        for block_left, block_right, shard_left, shard_right in pending:
            part_left = block_logits(block_left, shard_left)
            part_right = block_logits(block_right, shard_right)
            if logits_left is None:
                logits_left, logits_right = part_left, part_right
            else:
                logits_left = logits_left + part_left
                logits_right = logits_right + part_right
        return logits_left, logits_right

    for step in range(1, n_row):
        if step == 3:
            left, right, full_gain = lax.optimization_barrier((left, right, full_gain))
        if step == 5:
            stream = full_hidden.astype(jnp.float32)
            mean_square = jnp.sum(stream * stream, axis=2) / D
            features = (
                stream * lax.rsqrt(mean_square[:, :, None] + EPS) * full_gain[None, :, :]
            ).astype(jnp.bfloat16)
            left, right, features = lax.optimization_barrier((left, right, features))
            features = features.reshape(tok_rows, 2, n_row, shard_rows).transpose(2, 0, 1, 3)
        if step >= n_row - 2:
            newest = pending[-1]
            pending = pending[:-1]
            logits_left, logits_right = add_pending(logits_left, logits_right)
            pending = [newest]
            left, right, logits_left, logits_right = lax.optimization_barrier(
                (left, right, logits_left, logits_right)
            )
        left, right = lax.optimization_barrier((left, right))
        left = lax.ppermute(left, "row", forward)
        right = lax.ppermute(right, "row", backward)
        pending.append((left, right, (row_index - step) % n_row, (row_index + step) % n_row))
    logits_left, logits_right = add_pending(logits_left, logits_right)
    logits = jnp.concatenate([logits_left, logits_right], axis=2)
    row_max = jnp.max(logits, axis=2)
    exp_total = jnp.sum(jnp.exp(logits - row_max[:, :, None]), axis=2)
    vocab_ids = col_index * vocab_cols + jnp.arange(vocab_cols, dtype=jnp.int32)
    picked = jnp.sum(
        jnp.where(targets[:, None, None] == vocab_ids[None, None, :], logits, 0.0), axis=2
    )
    parts = lax.all_gather(jnp.stack([row_max, exp_total, picked]), "col")
    max_logit = jnp.max(parts[:, 0], axis=0)
    exp_total = jnp.sum(parts[:, 1] * jnp.exp(parts[:, 0] - max_logit[None]), axis=0)
    picked = jnp.sum(parts[:, 2], axis=0)
    logp = picked - (max_logit + jnp.log(exp_total))
    log_ratio = logp[:, 0] - logp[:, 1]
    token_index = row_index * tok_rows + jnp.arange(tok_rows, dtype=jnp.int32)
    seq_ends = jnp.cumsum(lengths)
    segment = jnp.sum((seq_ends[None, :] <= token_index[:, None]).astype(jnp.int32), axis=1)
    member = segment[:, None] == jnp.arange(lengths.shape[0], dtype=jnp.int32)[None, :]
    ratio_sums = jnp.sum(jnp.where(member, log_ratio[:, None], 0.0), axis=0)
    squares = jnp.sum(jnp.where(member, (log_ratio * log_ratio)[:, None], 0.0), axis=0)
    ratio_max = jnp.max(jnp.where(member, log_ratio[:, None], -1e30), axis=0)
    stats = lax.all_gather(jnp.stack([ratio_sums, squares, ratio_max]), "row")
    seq_stats = jnp.stack(
        [jnp.sum(stats[:, 0], axis=0), jnp.sum(stats[:, 1], axis=0), jnp.max(stats[:, 2], axis=0)]
    )
    owned = owner == col_index
    return jnp.where(owned[None, :], seq_stats, 0.0)[None]


def solution(mesh):
    in_specs = (P("row", None, "col"), P(None, "col"), P("row", "col"), P(), P("row"), P())
    out_specs = P("col", None, None)
    return jax.shard_map(
        per_device, mesh=mesh, in_specs=in_specs, out_specs=out_specs, check_vma=False
    )
```

```python
import jax
import jax.numpy as jnp
from jax import lax
from jax.sharding import PartitionSpec as P

D = 7168


EPS = 1e-05


def per_device(hidden_in, final_gain, unembed, lengths, targets, owner):
    tok_rows = hidden_in.shape[0]
    shard_rows, vocab_cols = unembed.shape
    half = vocab_cols // 2
    n_row = lax.axis_size("row")
    col_index = lax.axis_index("col")
    row_index = lax.axis_index("row")
    full_hidden = lax.all_gather(hidden_in, "col", axis=2, tiled=True)
    full_gain = lax.all_gather(final_gain, "col", axis=1, tiled=True)
    forward = [(i, (i + 1) % n_row) for i in range(n_row)]
    backward = [(i, (i - 1) % n_row) for i in range(n_row)]
    left, right = unembed[:, :half], unembed[:, half:]
    pending = [(left, right, row_index, row_index)]
    features = None
    logits_left = None
    logits_right = None

    def block_logits(block, shard):
        return jnp.einsum("tmd,dv->tmv", features[shard], block, preferred_element_type=jnp.float32)

    def add_pending(logits_left, logits_right):
        for block_left, block_right, shard_left, shard_right in pending:
            part_left = block_logits(block_left, shard_left)
            part_right = block_logits(block_right, shard_right)
            if logits_left is None:
                logits_left, logits_right = part_left, part_right
            else:
                logits_left = logits_left + part_left
                logits_right = logits_right + part_right
        return logits_left, logits_right

    for step in range(1, n_row):
        if step == 3:
            left, right, full_gain = lax.optimization_barrier((left, right, full_gain))
        if step == 5:
            stream = full_hidden.astype(jnp.float32)
            mean_square = jnp.sum(stream * stream, axis=2) / D
            features = (
                stream * lax.rsqrt(mean_square[:, :, None] + EPS) * full_gain[None, :, :]
            ).astype(jnp.bfloat16)
            left, right, features = lax.optimization_barrier((left, right, features))
            features = features.reshape(tok_rows, 2, n_row, shard_rows).transpose(2, 0, 1, 3)
        if step >= n_row - 2:
            newest = pending[-1]
            pending = pending[:-1]
            logits_left, logits_right = add_pending(logits_left, logits_right)
            pending = [newest]
            left, right, logits_left, logits_right = lax.optimization_barrier(
                (left, right, logits_left, logits_right)
            )
        left, right = lax.optimization_barrier((left, right))
        left = lax.ppermute(left, "row", forward)
        right = lax.ppermute(right, "row", backward)
        pending.append((left, right, (row_index - step) % n_row, (row_index + step) % n_row))
    logits_left, logits_right = add_pending(logits_left, logits_right)
    logits = jnp.concatenate([logits_left, logits_right], axis=2)
    row_max = jnp.max(logits, axis=2)
    exp_total = jnp.sum(jnp.exp(logits - row_max[:, :, None]), axis=2)
    vocab_ids = col_index * vocab_cols + jnp.arange(vocab_cols, dtype=jnp.int32)
    picked = jnp.sum(
        jnp.where(targets[:, None, None] == vocab_ids[None, None, :], logits, 0.0), axis=2
    )
    parts = lax.all_gather(jnp.stack([row_max, exp_total, picked]), "col")
    max_logit = jnp.max(parts[:, 0], axis=0)
    exp_total = jnp.sum(parts[:, 1] * jnp.exp(parts[:, 0] - max_logit[None]), axis=0)
    picked = jnp.sum(parts[:, 2], axis=0)
    logp = picked - (max_logit + jnp.log(exp_total))
    log_ratio = logp[:, 0] - logp[:, 1]
    token_index = row_index * tok_rows + jnp.arange(tok_rows, dtype=jnp.int32)
    seq_ends = jnp.cumsum(lengths)
    segment = jnp.sum((seq_ends[None, :] <= token_index[:, None]).astype(jnp.int32), axis=1)
    member = segment[:, None] == jnp.arange(lengths.shape[0], dtype=jnp.int32)[None, :]
    ratio_sums = jnp.sum(jnp.where(member, log_ratio[:, None], 0.0), axis=0)
    squares = jnp.sum(jnp.where(member, (log_ratio * log_ratio)[:, None], 0.0), axis=0)
    ratio_max = jnp.max(jnp.where(member, log_ratio[:, None], -1e30), axis=0)
    seq_stats = jnp.stack([ratio_sums, squares, ratio_max])
    distance = 1
    while distance < n_row:
        partner = [(i, i ^ distance) for i in range(n_row)]
        other = lax.ppermute(seq_stats, "row", partner)
        seq_stats = jnp.stack(
            [
                seq_stats[0] + other[0],
                seq_stats[1] + other[1],
                jnp.maximum(seq_stats[2], other[2]),
            ]
        )
        distance *= 2
    owned = owner == col_index
    return jnp.where(owned[None, :], seq_stats, 0.0)[None]


def solution(mesh):
    in_specs = (P("row", None, "col"), P(None, "col"), P("row", "col"), P(), P("row"), P())
    out_specs = P("col", None, None)
    return jax.shard_map(
        per_device, mesh=mesh, in_specs=in_specs, out_specs=out_specs, check_vma=False
    )
```

```python
import jax
import jax.numpy as jnp
from jax import lax
from jax.sharding import PartitionSpec as P

D = 7168


EPS = 1e-05


def per_device(hidden_in, final_gain, unembed, lengths, targets, owner):
    tok_rows = hidden_in.shape[0]
    shard_rows, vocab_cols = unembed.shape
    half = vocab_cols // 2
    n_row = lax.axis_size("row")
    col_index = lax.axis_index("col")
    row_index = lax.axis_index("row")
    full_hidden = lax.all_gather(hidden_in, "col", axis=2, tiled=True)
    full_gain = lax.all_gather(final_gain, "col", axis=1, tiled=True)
    forward = [(i, (i + 1) % n_row) for i in range(n_row)]
    backward = [(i, (i - 1) % n_row) for i in range(n_row)]
    left, right = unembed[:, :half], unembed[:, half:]
    pending = [(left, right, row_index, row_index)]
    features = None
    logits_left = None
    logits_right = None

    def block_logits(block, shard):
        return jnp.einsum("tmd,dv->tmv", features[shard], block, preferred_element_type=jnp.float32)

    def add_pending(logits_left, logits_right):
        for block_left, block_right, shard_left, shard_right in pending:
            part_left = block_logits(block_left, shard_left)
            part_right = block_logits(block_right, shard_right)
            if logits_left is None:
                logits_left, logits_right = part_left, part_right
            else:
                logits_left = logits_left + part_left
                logits_right = logits_right + part_right
        return logits_left, logits_right

    for step in range(1, n_row):
        if step == 3:
            left, right, full_gain = lax.optimization_barrier((left, right, full_gain))
        if step == 5:
            stream = full_hidden.astype(jnp.float32)
            mean_square = jnp.sum(stream * stream, axis=2) / D
            features = (
                stream * lax.rsqrt(mean_square[:, :, None] + EPS) * full_gain[None, :, :]
            ).astype(jnp.bfloat16)
            left, right, features = lax.optimization_barrier((left, right, features))
            features = features.reshape(tok_rows, 2, n_row, shard_rows).transpose(2, 0, 1, 3)
        if step >= n_row - 2:
            newest = pending[-1]
            pending = pending[:-1]
            logits_left, logits_right = add_pending(logits_left, logits_right)
            pending = [newest]
            left, right, logits_left, logits_right = lax.optimization_barrier(
                (left, right, logits_left, logits_right)
            )
        left, right = lax.optimization_barrier((left, right))
        left = lax.ppermute(left, "row", forward)
        right = lax.ppermute(right, "row", backward)
        pending.append((left, right, (row_index - step) % n_row, (row_index + step) % n_row))
    logits_left, logits_right = add_pending(logits_left, logits_right)
    logits = jnp.concatenate([logits_left, logits_right], axis=2)
    row_max = jnp.max(logits, axis=2)
    exp_total = jnp.sum(jnp.exp(logits - row_max[:, :, None]), axis=2)
    vocab_ids = col_index * vocab_cols + jnp.arange(vocab_cols, dtype=jnp.int32)
    picked = jnp.sum(
        jnp.where(targets[:, None, None] == vocab_ids[None, None, :], logits, 0.0), axis=2
    )
    n_col = lax.axis_size("col")
    max_logit = row_max
    distance = 1
    while distance < n_col:
        partner = [(i, i ^ distance) for i in range(n_col)]
        other = lax.ppermute(jnp.stack([max_logit, exp_total, picked]), "col", partner)
        joint_max = jnp.maximum(max_logit, other[0])
        exp_total = exp_total * jnp.exp(max_logit - joint_max) + other[1] * jnp.exp(
            other[0] - joint_max
        )
        picked = picked + other[2]
        max_logit = joint_max
        distance *= 2
    logp = picked - (max_logit + jnp.log(exp_total))
    log_ratio = logp[:, 0] - logp[:, 1]
    token_index = row_index * tok_rows + jnp.arange(tok_rows, dtype=jnp.int32)
    seq_ends = jnp.cumsum(lengths)
    segment = jnp.sum((seq_ends[None, :] <= token_index[:, None]).astype(jnp.int32), axis=1)
    member = segment[:, None] == jnp.arange(lengths.shape[0], dtype=jnp.int32)[None, :]
    ratio_sums = jnp.sum(jnp.where(member, log_ratio[:, None], 0.0), axis=0)
    squares = jnp.sum(jnp.where(member, (log_ratio * log_ratio)[:, None], 0.0), axis=0)
    ratio_max = jnp.max(jnp.where(member, log_ratio[:, None], -1e30), axis=0)
    seq_stats = jnp.stack([ratio_sums, squares, ratio_max])
    distance = 1
    while distance < n_row:
        partner = [(i, i ^ distance) for i in range(n_row)]
        other = lax.ppermute(seq_stats, "row", partner)
        seq_stats = jnp.stack(
            [
                seq_stats[0] + other[0],
                seq_stats[1] + other[1],
                jnp.maximum(seq_stats[2], other[2]),
            ]
        )
        distance *= 2
    owned = owner == col_index
    return jnp.where(owned[None, :], seq_stats, 0.0)[None]


def solution(mesh):
    in_specs = (P("row", None, "col"), P(None, "col"), P("row", "col"), P(), P("row"), P())
    out_specs = P("col", None, None)
    return jax.shard_map(
        per_device, mesh=mesh, in_specs=in_specs, out_specs=out_specs, check_vma=False
    )
```

```python
import jax
import jax.numpy as jnp
from jax import lax
from jax.sharding import PartitionSpec as P

D = 7168


EPS = 1e-05


def per_device(hidden_in, final_gain, unembed, lengths, targets, owner):
    tok_rows = hidden_in.shape[0]
    shard_rows, vocab_cols = unembed.shape
    half = vocab_cols // 2
    n_row = lax.axis_size("row")
    col_index = lax.axis_index("col")
    row_index = lax.axis_index("row")
    full_hidden = lax.all_gather(hidden_in, "col", axis=2, tiled=True)
    n_col = lax.axis_size("col")
    full_gain = final_gain
    distance = 1
    while distance < n_col:
        partner = [(i, i ^ distance) for i in range(n_col)]
        other = lax.ppermute(full_gain, "col", partner)
        lower = (col_index // distance) % 2 == 0
        full_gain = jnp.where(
            lower,
            jnp.concatenate([full_gain, other], axis=1),
            jnp.concatenate([other, full_gain], axis=1),
        )
        distance *= 2
    forward = [(i, (i + 1) % n_row) for i in range(n_row)]
    backward = [(i, (i - 1) % n_row) for i in range(n_row)]
    left, right = unembed[:, :half], unembed[:, half:]
    pending = [(left, right, row_index, row_index)]
    features = None
    logits_left = None
    logits_right = None

    def block_logits(block, shard):
        return jnp.einsum("tmd,dv->tmv", features[shard], block, preferred_element_type=jnp.float32)

    def add_pending(logits_left, logits_right):
        for block_left, block_right, shard_left, shard_right in pending:
            part_left = block_logits(block_left, shard_left)
            part_right = block_logits(block_right, shard_right)
            if logits_left is None:
                logits_left, logits_right = part_left, part_right
            else:
                logits_left = logits_left + part_left
                logits_right = logits_right + part_right
        return logits_left, logits_right

    for step in range(1, n_row):
        if step == 3:
            left, right, full_gain = lax.optimization_barrier((left, right, full_gain))
        if step == 5:
            stream = full_hidden.astype(jnp.float32)
            mean_square = jnp.sum(stream * stream, axis=2) / D
            features = (
                stream * lax.rsqrt(mean_square[:, :, None] + EPS) * full_gain[None, :, :]
            ).astype(jnp.bfloat16)
            left, right, features = lax.optimization_barrier((left, right, features))
            features = features.reshape(tok_rows, 2, n_row, shard_rows).transpose(2, 0, 1, 3)
        if step >= n_row - 2:
            newest = pending[-1]
            pending = pending[:-1]
            logits_left, logits_right = add_pending(logits_left, logits_right)
            pending = [newest]
            left, right, logits_left, logits_right = lax.optimization_barrier(
                (left, right, logits_left, logits_right)
            )
        left, right = lax.optimization_barrier((left, right))
        left = lax.ppermute(left, "row", forward)
        right = lax.ppermute(right, "row", backward)
        pending.append((left, right, (row_index - step) % n_row, (row_index + step) % n_row))
    logits_left, logits_right = add_pending(logits_left, logits_right)
    logits = jnp.concatenate([logits_left, logits_right], axis=2)
    row_max = jnp.max(logits, axis=2)
    exp_total = jnp.sum(jnp.exp(logits - row_max[:, :, None]), axis=2)
    vocab_ids = col_index * vocab_cols + jnp.arange(vocab_cols, dtype=jnp.int32)
    picked = jnp.sum(
        jnp.where(targets[:, None, None] == vocab_ids[None, None, :], logits, 0.0), axis=2
    )
    max_logit = row_max
    distance = 1
    while distance < n_col:
        partner = [(i, i ^ distance) for i in range(n_col)]
        other = lax.ppermute(jnp.stack([max_logit, exp_total, picked]), "col", partner)
        joint_max = jnp.maximum(max_logit, other[0])
        exp_total = exp_total * jnp.exp(max_logit - joint_max) + other[1] * jnp.exp(
            other[0] - joint_max
        )
        picked = picked + other[2]
        max_logit = joint_max
        distance *= 2
    logp = picked - (max_logit + jnp.log(exp_total))
    log_ratio = logp[:, 0] - logp[:, 1]
    token_index = row_index * tok_rows + jnp.arange(tok_rows, dtype=jnp.int32)
    seq_ends = jnp.cumsum(lengths)
    segment = jnp.sum((seq_ends[None, :] <= token_index[:, None]).astype(jnp.int32), axis=1)
    member = segment[:, None] == jnp.arange(lengths.shape[0], dtype=jnp.int32)[None, :]
    ratio_sums = jnp.sum(jnp.where(member, log_ratio[:, None], 0.0), axis=0)
    squares = jnp.sum(jnp.where(member, (log_ratio * log_ratio)[:, None], 0.0), axis=0)
    ratio_max = jnp.max(jnp.where(member, log_ratio[:, None], -1e30), axis=0)
    seq_stats = jnp.stack([ratio_sums, squares, ratio_max])
    distance = 1
    while distance < n_row:
        partner = [(i, i ^ distance) for i in range(n_row)]
        other = lax.ppermute(seq_stats, "row", partner)
        seq_stats = jnp.stack(
            [
                seq_stats[0] + other[0],
                seq_stats[1] + other[1],
                jnp.maximum(seq_stats[2], other[2]),
            ]
        )
        distance *= 2
    owned = owner == col_index
    return jnp.where(owned[None, :], seq_stats, 0.0)[None]


def solution(mesh):
    in_specs = (P("row", None, "col"), P(None, "col"), P("row", "col"), P(), P("row"), P())
    out_specs = P("col", None, None)
    return jax.shard_map(
        per_device, mesh=mesh, in_specs=in_specs, out_specs=out_specs, check_vma=False
    )
```
